32 devices in a mesh: grp: 2 (over x), chan: 16 (over z, y, core).
Axes of the slice: x: 2, y: 2, z: 4, core: 2. Of those that a mesh axis runs over, the one named last changes fastest.
Arguments:
- samples: bfloat16 [128, 62, 8192], P('chan', 'grp'), parts along dimension 1, may hold values from -6 to 6
- eq_gain: float32 [128, 4096], P('chan'), may hold values from 0.5 to 2
- delays: float32 [1024, 64], replicated, may hold values from -64 to 64
Outputs:
- beams: bfloat16 [2, 1024, 4096], P('grp', 'chan'), parts along dimension 0
The draws below stay inside these ranges and needn't reach their ends.
There are 2 independent parts, one for each index of `grp`. The reference program is written for one: setup_inputs(seed, part) draws one part's arguments, and reference() takes and returns one part's arrays. A program takes and returns all parts, laid end to end along the dimension named above; an argument that names none is the same for every part. Nothing has to cross between parts.
All inputs are finite; a program needn't handle non-finite values.
Results may differ from the reference program's by a relative error of at most 0.0034.
Values may be sent and summed in bfloat16 or wider, within the bound.
No kernel may reach another device: no remote copies, remote signals or barrier semaphores. Data moves between devices by JAX's collectives and lax.ppermute only.
A program may use at most 448 MiB of HBM per device.

```python
import math
import jax
import jax.numpy as jnp
from jax import lax

DISHES = 64
POLS = 2
NI = 128
NC = 4096
NB = 1024
TAPS = 16
AVG = 16
SPEC = 16
TA = 1
FRAMES = 31
FRAME = 8192


def block_levels(key, shape, pieces, least, largest):
    loudness, own = 1.0, jax.random.fold_in(key, 6)
    for dim, blocks in pieces:
        steps = jnp.exp(jax.random.uniform(jax.random.fold_in(own, dim), (blocks,), jnp.float32, least / len(pieces), largest / len(pieces)))
        loudness = loudness * jnp.repeat(steps, shape[dim] // blocks).reshape([-1 if axis == dim else 1 for axis in range(len(shape))])
    return loudness


def noise(rng, extent, width, most, split=(), held_as=jnp.bfloat16):
    values = width * jax.random.normal(rng, extent, jnp.float32)
    if split:
        values = values * block_levels(rng, extent, split, -0.22, 0.18)
    return jnp.clip(values, -most, most).astype(held_as)


def setup_inputs(seed: int = 0, part: int = 0) -> dict:
    arg_keys = jax.random.split(jax.random.key(seed), 4)
    part_splits = jax.random.split(jax.random.fold_in(arg_keys[3], part), 4)
    return {
        "samples": noise(part_splits[0], (NI, FRAMES, FRAME), 1.0, 6.0, ((0, 16),)),
        "eq_gain": jnp.clip(jnp.exp(math.log(2.0) - 1.3862944 * jax.random.uniform(arg_keys[1], (NI, NC), jnp.float32) ** block_levels(arg_keys[1], (NI, NC), ((0, 16),), -0.2, 0.2)), 0.5, 2.0),
        "delays": jnp.clip(jax.random.uniform(arg_keys[2], (NB, DISHES), jnp.float32, -64.0, 64.0), -64.0, 64.0),
    }


def pfb_taps(frame_len, tap_count):
    tap_total = tap_count * frame_len
    position = jnp.arange(tap_total, dtype=jnp.float32) + 0.5
    window = 0.5 - 0.5 * jnp.cos(2.0 * math.pi / tap_total * position)
    offset = (position - 0.5 * tap_total) / frame_len
    prototype = window * jnp.sin(math.pi * offset) / (math.pi * offset)
    prototype = prototype / jnp.sqrt(jnp.sum(prototype * prototype))
    return prototype.reshape(tap_count, frame_len)

def reference(samples, eq_gain, delays):
    frame_len = 2 * NC
    tap_table = pfb_taps(frame_len, TAPS)
    filtered = jnp.zeros((NI, SPEC, frame_len), jnp.float32)
    for tap_index in range(TAPS):
        filtered = filtered + tap_table[tap_index] * samples[:, tap_index:tap_index + SPEC, :].astype(jnp.float32)
    spectrum = jnp.fft.rfft(filtered, axis=-1)[:, :, :NC]
    gain_row = eq_gain[:, None, :]
    volt_real = (jnp.real(spectrum) * gain_row).astype(jnp.bfloat16)
    volt_imag = (jnp.imag(spectrum) * gain_row).astype(jnp.bfloat16)
    block_len = min(64, NC)
    block_count = NC // block_len
    real_blocks = jnp.moveaxis(volt_real.reshape(DISHES, POLS, SPEC, block_count, block_len), 3, 0)
    imag_blocks = jnp.moveaxis(volt_imag.reshape(DISHES, POLS, SPEC, block_count, block_len), 3, 0)
    starts = jnp.arange(block_count, dtype=jnp.int32) * block_len
    weight_scale = 1.0 / math.sqrt(DISHES)

    def one_block(block_args):
        real_part, imag_part, start = block_args
        channel = (start + jnp.arange(block_len, dtype=jnp.int32)).astype(jnp.float32)
        phase_turns = channel[:, None, None] * delays[None, :, :] / frame_len
        phase_angle = 2.0 * math.pi * phase_turns
        w_real = lax.optimization_barrier((jnp.cos(phase_angle) * weight_scale).astype(jnp.bfloat16)).astype(jnp.float32)
        w_imag = lax.optimization_barrier((-jnp.sin(phase_angle) * weight_scale).astype(jnp.bfloat16)).astype(jnp.float32)
        v_real = real_part.astype(jnp.float32)
        v_imag = imag_part.astype(jnp.float32)
        beam_real = jnp.einsum('cbd,dpsc->cbps', w_real, v_real) - jnp.einsum('cbd,dpsc->cbps', w_imag, v_imag)
        beam_imag = jnp.einsum('cbd,dpsc->cbps', w_real, v_imag) + jnp.einsum('cbd,dpsc->cbps', w_imag, v_real)
        energy = beam_real * beam_real + beam_imag * beam_imag
        energy = lax.optimization_barrier(jnp.sum(energy.reshape(block_len, NB, POLS, TA, AVG), axis=(2, 4))) / AVG
        return energy.astype(jnp.bfloat16)
    result = lax.map(one_block, (real_blocks, imag_blocks, starts))
    return result.reshape(NC, NB, TA).transpose(2, 1, 0)
```

```python
import math

import jax
import jax.numpy as jnp
from jax import lax
from jax.sharding import PartitionSpec as P

DISHES = 64
POLS = 2
NB = 1024
TAPS = 16
AVG = 16
SPEC = 16


def pfb_taps(frame_len, tap_count):
    tap_total = tap_count * frame_len
    position = jnp.arange(tap_total, dtype=jnp.float32) + 0.5
    window = 0.5 - 0.5 * jnp.cos(2.0 * math.pi / tap_total * position)
    offset = (position - 0.5 * tap_total) / frame_len
    prototype = window * jnp.sin(math.pi * offset) / (math.pi * offset)
    prototype = prototype / jnp.sqrt(jnp.sum(prototype * prototype))
    return prototype.reshape(tap_count, frame_len)


def cos_sin(numer, denom):
    phase_angle = 2.0 * math.pi / denom * numer.astype(jnp.float32)
    return (jnp.cos(phase_angle), -jnp.sin(phase_angle))


def turn_tables(frame_len):
    outer_len = 2 ** ((frame_len.bit_length() - 1) // 2)
    inner_len = frame_len // outer_len
    half_len = inner_len // 2
    outer_index = jnp.arange(outer_len, dtype=jnp.int32)
    inner_index = jnp.arange(inner_len, dtype=jnp.int32)
    half_index = jnp.arange(half_len, dtype=jnp.int32)
    one_cos, one_sin = cos_sin(outer_index[:, None] * outer_index[None, :] % outer_len, outer_len)
    twist_cos, twist_sin = cos_sin(
        outer_index[:, None] * inner_index[None, :] % frame_len, frame_len
    )
    three_cos, three_sin = cos_sin(
        inner_index[:, None] * half_index[None, :] % inner_len, inner_len
    )
    table_one = jnp.stack([one_cos, one_sin])
    table_three = jnp.stack([three_cos, three_sin])
    return (outer_len, inner_len, table_one, twist_cos, twist_sin, table_three)


def body(samples, eq_gain, delays):
    inputs_here, frame_count, frame_len = samples.shape
    chan_count = frame_len // 2
    groups = lax.axis_size("chan")
    my_index = lax.axis_index("chan")
    chan_here = chan_count // groups
    beams_here = NB // groups
    time_bins = SPEC // AVG
    highest = lax.Precision.HIGHEST
    tap_table = pfb_taps(frame_len, TAPS)
    filtered = jnp.zeros((inputs_here, SPEC, frame_len), jnp.float32)
    for tap_index in range(TAPS):
        filtered = filtered + tap_table[tap_index] * samples[
            :, tap_index : tap_index + SPEC, :
        ].astype(jnp.float32)
    outer_len, inner_len, table_one, twist_cos, twist_sin, table_three = turn_tables(frame_len)
    framed = filtered.reshape(inputs_here, SPEC, outer_len, inner_len)
    section_one = jnp.einsum("rkn,isnm->irskm", table_one, framed, precision=highest)
    real_one = section_one[:, 0]
    imag_one = section_one[:, 1]
    twisted = jnp.stack(
        [real_one * twist_cos - imag_one * twist_sin, real_one * twist_sin + imag_one * twist_cos],
        axis=1,
    )
    section_three = jnp.einsum("irskm,qmj->irqsjk", twisted, table_three, precision=highest)
    spec_real = (section_three[:, 0, 0] - section_three[:, 1, 1]).reshape(
        inputs_here, SPEC, chan_count
    )
    spec_imag = (section_three[:, 0, 1] + section_three[:, 1, 0]).reshape(
        inputs_here, SPEC, chan_count
    )
    gain_row = eq_gain[:, None, :]
    volt_real = (spec_real * gain_row).astype(jnp.bfloat16)
    volt_imag = (spec_imag * gain_row).astype(jnp.bfloat16)
    outgoing = jnp.stack([volt_real, volt_imag], axis=1).transpose(3, 1, 2, 0)
    arrived = lax.all_to_all(outgoing, "chan", split_axis=0, concat_axis=3, tiled=True)
    dish_volts = arrived.reshape(chan_here, 2, SPEC, DISHES, POLS).transpose(0, 1, 4, 2, 3)
    real_part = dish_volts[:, 0]
    imag_part = dish_volts[:, 1]
    volt_operand = jnp.stack(
        [
            jnp.concatenate([real_part, -imag_part], axis=-1),
            jnp.concatenate([imag_part, real_part], axis=-1),
        ],
        axis=1,
    ).reshape(chan_here, 2 * POLS * SPEC, 2 * DISHES)
    low_len = math.gcd(chan_here, 2 ** ((chan_here.bit_length() - 1) // 2))
    high_count = chan_here // low_len
    weight_scale = 1.0 / math.sqrt(DISHES)

    def rotation(channel, scale):
        turns = channel.astype(jnp.float32)[:, None, None] * delays[None, :, :] / frame_len
        turns = turns - jnp.round(turns)
        angle = 2.0 * math.pi * turns
        return jnp.cos(angle) * scale, -jnp.sin(angle) * scale

    high_channel = my_index * chan_here + jnp.arange(high_count, dtype=jnp.int32) * low_len
    high_real, high_imag = rotation(high_channel, weight_scale)
    low_real, low_imag = rotation(jnp.arange(low_len, dtype=jnp.int32), 1.0)
    volt_blocks = volt_operand.reshape(high_count, low_len, 2 * POLS * SPEC, 2 * DISHES)

    def one_block(block_args):
        base_real, base_imag, volt_part = block_args
        w_real = (base_real * low_real - base_imag * low_imag).astype(jnp.bfloat16)
        w_imag = (base_real * low_imag + base_imag * low_real).astype(jnp.bfloat16)
        weight_part = jnp.concatenate([w_real, w_imag], axis=-1)
        product = jnp.einsum(
            "cnk,cbk->cnb", volt_part, weight_part, preferred_element_type=jnp.float32
        ).reshape(low_len, 2 * POLS, time_bins, AVG, NB)
        return jnp.sum(product * product, axis=(1, 3)) / AVG

    energy = lax.map(one_block, (high_real, high_imag, volt_blocks))
    power_bins = (
        energy.reshape(chan_here, time_bins, NB).transpose(1, 2, 0).astype(jnp.bfloat16)
    )
    return lax.all_to_all(power_bins, "chan", split_axis=1, concat_axis=2, tiled=True)


def solution(mesh):
    in_specs = (P("chan", "grp", None), P("chan", None), P())
    out_specs = P("grp", "chan", None)
    return jax.shard_map(body, mesh=mesh, in_specs=in_specs, out_specs=out_specs, check_vma=False)
```
